512 devices in a mesh: segment: 4 (over z_lo), seq: 16 (over z_hi, x, core), mp: 8 (over y).
Axes of the slice: x: 4, y: 8, z: 8 (z_hi: 2, z_lo: 4; z = z_hi * 4 + z_lo), core: 2. Of those that a mesh axis runs over, the one named last changes fastest.
Arguments:
- latents: bfloat16 [4, 16, 256, 4096], P('segment', 'seq', None, 'mp'), may hold values from -6 to 6
- w_qkv: bfloat16 [4, 4096, 3, 4096], P('segment', 'seq', None, 'mp'), may hold values from -1 to 1
- w_out: bfloat16 [4, 4096, 4096], P('segment', 'mp', 'seq'), may hold values from -0.09375 to 0.09375
- mod_shift: float32 [4, 4096], P('segment'), may hold values from -3 to 3
- mod_scale: float32 [4, 4096], P('segment'), may hold values from 0.1 to 1.9
- mod_gate: float32 [4, 4096], P('segment'), may hold values from 0.5 to 1.5
- counts: int32 [4, 16], P('segment'), may hold values from 64 to 256, as said below
Outputs:
- next_latents: bfloat16 [4, 16, 256, 4096], P('segment', 'seq', None, 'mp')
The draws below stay inside these ranges and needn't reach their ends.
Inputs may be any that keep to these rules, and one draw needn't show every extreme that they name: `counts`: in every section's clip at least one frame has all 256 patch positions valid.
All inputs are finite; a program needn't handle non-finite values.
Results may differ from the reference program's by a relative error of at most 0.01.
Values may be sent and summed in bfloat16 or wider, within the bound.
No kernel may reach another device: no remote copies, remote signals or barrier semaphores. Data moves between devices by JAX's collectives and lax.ppermute only.
A program may use at most 64 MiB of HBM per device.

```python
import math
import jax
import jax.numpy as jnp
from jax import lax

D = 4096
HEADS = 32
HD = 128
P_SIZE = 256
FRAMES = 16
SEGMENTS = 4
N_MP = 8


def draw_latents(key, part):
    shape = (SEGMENTS, FRAMES, P_SIZE, D)
    return jnp.clip(jax.random.normal(jax.random.fold_in(key, 23), shape, dtype=jnp.float32), -6.0, 6.0).astype(jnp.bfloat16)


def draw_w_qkv(key, part):
    shape = (SEGMENTS, D, 3, HEADS * HD)
    return (jnp.clip(jax.random.normal(jax.random.fold_in(key, 33), shape, dtype=jnp.float32), -5.0, 5.0) / math.sqrt(D)).astype(jnp.bfloat16)


def draw_counts(key, part):
    base = jax.random.randint(jax.random.fold_in(key, 3), (SEGMENTS, FRAMES), P_SIZE // 4, P_SIZE + 1)
    full_frame = jax.random.randint(jax.random.fold_in(key, 5), (SEGMENTS, 1), 0, FRAMES)
    return jnp.where(jnp.arange(FRAMES)[None, :] == full_frame, P_SIZE, base).astype(jnp.int32)


def level_of(stream_key, dims, pieces, least, largest):
    def one(axis_at, shards_of):
        draws = jax.random.uniform(jax.random.fold_in(jax.random.fold_in(stream_key, 6), axis_at), (shards_of,), jnp.float32, least / len(pieces), largest / len(pieces))
        return jnp.repeat(jnp.exp(draws), dims[axis_at] // shards_of).reshape((-1,) + (1,) * (len(dims) - axis_at - 1))

    level = one(*pieces[0])
    for cut in pieces[1:]:
        level = level * one(*cut)
    return level


def scatter_about(rng, extent, scale, most, cuts=(), kind=jnp.bfloat16):
    loudness = level_of(rng, extent, cuts, -0.22, 0.18) if cuts else 1.0
    drawn = jax.random.normal(rng, extent, jnp.float32) * scale * loudness
    return jnp.minimum(jnp.maximum(drawn, -most), most).astype(kind)


def setup_inputs(seed: int = 0) -> dict:
    keys = jax.random.split(jax.random.key(seed), 8)
    return {
        "latents": draw_latents(jax.random.fold_in(keys[7], 71), 0),
        "w_qkv": draw_w_qkv(jax.random.fold_in(keys[7], 71), 0),
        "w_out": scatter_about(keys[2], (SEGMENTS, HEADS * HD, D), (HEADS * HD) ** -0.5, 0.09375, ((0, 4), (1, 8), (2, 16))),
        "mod_shift": scatter_about(keys[3], (SEGMENTS, D), 0.5, 3.0, ((0, 4),), jnp.float32),
        "mod_scale": jnp.clip(1.0 + 0.18 * jax.random.normal(keys[4], (SEGMENTS, D), jnp.float32), 0.1, 1.9),
        "mod_gate": jnp.clip(0.5 + 1.0 * jax.random.uniform(keys[5], (SEGMENTS, D), jnp.float32) ** level_of(keys[5], (SEGMENTS, D), ((0, 4),), -0.2, 0.2), 0.5, 1.5),
        "counts": draw_counts(jax.random.fold_in(keys[7], 71), 0),
    }


EPS = 1e-06
NEG_FILL = -1e+30

def masked_attention(queries, keys_in, values, usable):
    factor = 1.0 / math.sqrt(queries.shape[-1])
    scores = jnp.einsum('...ihe,...jhe->...hij', queries.astype(jnp.float32), keys_in.astype(jnp.float32)) * factor
    allowed = usable[..., None, :, None] & usable[..., None, None, :]
    masked = jnp.where(allowed, scores, NEG_FILL)
    highest = lax.optimization_barrier(jnp.max(masked, axis=-1, keepdims=True))
    raised = jnp.where(allowed, jnp.exp(masked - highest), 0.0)
    spare_one = jnp.where(usable, 0.0, 1.0)[..., None, :, None]
    weights = (raised / (lax.optimization_barrier(jnp.sum(raised, axis=-1, keepdims=True)) + spare_one)).astype(jnp.bfloat16)
    blended = jnp.einsum('...hij,...jhe->...ihe', weights.astype(jnp.float32), values.astype(jnp.float32))
    return blended.astype(jnp.bfloat16)

def section(block_rows, w_in, w_proj, shift_vec, scale_vec, gate_vec, clip_counts, spatial):
    frames = block_rows.shape[0]
    patches = block_rows.shape[1]
    span = patches // frames
    widened = block_rows.astype(jnp.float32)
    average = lax.optimization_barrier(jnp.mean(widened, axis=-1, keepdims=True))
    centred = widened - average
    variance = lax.optimization_barrier(jnp.mean(centred * centred, axis=-1, keepdims=True))
    modulated = (centred * lax.rsqrt(variance + EPS) * scale_vec + shift_vec).astype(jnp.bfloat16)
    projected = jnp.dot(modulated.reshape(-1, D), w_in.reshape(D, -1), preferred_element_type=jnp.float32)
    projected = projected.astype(jnp.bfloat16).reshape(frames, patches, 3, HEADS, HD)
    if spatial:
        usable = jnp.arange(patches)[None, :] < clip_counts[:, None]
        attended = lax.map(lambda member: masked_attention(member[0], member[1], member[2], member[3]), (projected[:, :, 0], projected[:, :, 1], projected[:, :, 2], usable))
    else:
        by_place = projected.reshape(frames, frames, span, 3, HEADS, HD).transpose(0, 2, 1, 3, 4, 5)
        location = jnp.arange(frames)[:, None] * span + jnp.arange(span)[None, :]
        usable = location[:, :, None] < clip_counts[None, None, :]
        attended = masked_attention(by_place[:, :, :, 0], by_place[:, :, :, 1], by_place[:, :, :, 2], usable)
        attended = attended.transpose(0, 2, 1, 3, 4)
    attended = attended.reshape(frames * patches, HEADS * HD)
    per_group = HEADS * HD // N_MP
    branch = jnp.zeros((frames * patches, D), jnp.float32)
    for member in range(N_MP):
        partial_value = jnp.dot(attended[:, member * per_group:(member + 1) * per_group], w_proj[member * per_group:(member + 1) * per_group], preferred_element_type=jnp.float32)
        rounded = lax.optimization_barrier(partial_value.astype(jnp.bfloat16))
        branch = branch + rounded.astype(jnp.float32)
    updated = (widened.reshape(-1, D) + gate_vec * branch).astype(jnp.bfloat16)
    return updated.reshape(frames, frames, span, D).transpose(1, 0, 2, 3).reshape(frames, patches, D)

def reference(latents, w_qkv, w_out, mod_shift, mod_scale, mod_gate, counts):
    results = []
    for section_id in range(SEGMENTS):
        results.append(section(latents[section_id], w_qkv[section_id], w_out[section_id], mod_shift[section_id], mod_scale[section_id], mod_gate[section_id], counts[section_id], section_id % 2 == 0))
    moved = [results[(member - 1) % SEGMENTS] for member in range(SEGMENTS)]
    return jnp.stack(moved)
```

```python
import math

import jax
import jax.numpy as jnp
from jax import lax
from jax.sharding import PartitionSpec as P

HD = 128


EPS = 1e-06
NEG_FILL = -1e30


def passed_along(x, axis, by):
    length = lax.axis_size(axis)
    return lax.ppermute(x, axis, [(i, (i + by) % length) for i in range(length)])


def masked_attention(queries, keys_in, values, usable):
    factor = 1.0 / math.sqrt(queries.shape[-1])
    scores = (
        jnp.einsum("...ihe,...jhe->...hij", queries, keys_in, preferred_element_type=jnp.float32)
        * factor
    )
    allowed = usable[..., None, :, None] & usable[..., None, None, :]
    masked = jnp.where(allowed, scores, NEG_FILL)
    highest = jnp.max(masked, axis=-1, keepdims=True)
    raised = jnp.where(allowed, jnp.exp(masked - highest), 0.0)
    spare_one = jnp.where(usable, 0.0, 1.0)[..., None, :, None]
    weights = (raised / (jnp.sum(raised, axis=-1, keepdims=True) + spare_one)).astype(jnp.bfloat16)
    blended = jnp.einsum(
        "...hij,...jhe->...ihe", weights, values, preferred_element_type=jnp.float32
    )
    return blended.astype(jnp.bfloat16)


SEQ = ("zh", "x", "c")


def seq_index():
    return (lax.axis_index("zh") * lax.axis_size("x") + lax.axis_index("x")) * lax.axis_size(
        "c"
    ) + lax.axis_index("c")


def gather_seq(block):
    across = lax.all_gather(block, "zh", axis=0)
    along = lax.all_gather(across, "x", axis=1)
    both = lax.all_gather(along, "c", axis=2)
    return both.reshape((-1,) + block.shape[1:])


def relay_features(rows_now):
    return lax.all_to_all(rows_now, SEQ, split_axis=0, concat_axis=0, tiled=True)


def pass_onward(rows_now):
    return passed_along(rows_now, "segment", 1)


def on_device(latents, w_qkv, w_out, mod_shift, mod_scale, mod_gate, counts):
    frames = lax.axis_size(SEQ)
    patches = latents.shape[2]
    narrow = latents.shape[3]
    span = patches // frames
    segment_rows = latents[0, 0]
    gathered = lax.all_gather(latents, "mp", axis=3, tiled=True)[0, 0]
    widened = gathered.astype(jnp.float32)
    average = jnp.mean(widened, axis=-1, keepdims=True)
    centred = widened - average
    variance = jnp.mean(centred * centred, axis=-1, keepdims=True)
    modulated = (centred * lax.rsqrt(variance + EPS) * mod_scale[0] + mod_shift[0]).astype(
        jnp.bfloat16
    )
    columns = w_qkv.shape[2] * w_qkv.shape[3]
    piece = gather_seq(w_qkv[0])
    height = piece.shape[0]
    projected = jnp.dot(
        modulated, piece.reshape(height, columns), preferred_element_type=jnp.float32
    )
    local_heads = w_qkv.shape[3] // HD
    projected = projected.astype(jnp.bfloat16).reshape(patches, 3, local_heads, HD)
    frame_here = seq_index()
    clip_counts = counts[0]
    positions = jnp.arange(frames)

    def spatial(triple):
        count_here = jnp.sum(jnp.where(positions == frame_here, clip_counts, 0))
        usable = jnp.arange(patches) < count_here
        return masked_attention(triple[:, 0], triple[:, 1], triple[:, 2], usable)

    def temporal(triple):
        by_place = triple.reshape(frames, span, 3, local_heads, HD).transpose(1, 0, 2, 3, 4)
        location = frame_here * span + jnp.arange(span)
        usable = location[:, None] < clip_counts[None, :]
        blended = masked_attention(by_place[:, :, 0], by_place[:, :, 1], by_place[:, :, 2], usable)
        return blended.transpose(1, 0, 2, 3).reshape(patches, local_heads, HD)

    attended = lax.cond(lax.axis_index("segment") % 2 == 0, spatial, temporal, projected)
    attended = attended.reshape(patches, local_heads * HD)
    out_blocks = gather_seq(w_out[0][None])
    member = lax.axis_index("mp")
    partials = jnp.einsum(
        "tr,brc->tbc", attended, out_blocks, preferred_element_type=jnp.float32
    ).reshape(patches, -1)
    summed = lax.psum_scatter(
        partials.astype(jnp.bfloat16), "mp", scatter_dimension=1, tiled=True
    ).astype(jnp.float32)
    gate_here = lax.dynamic_slice_in_dim(mod_gate[0], member * narrow, narrow)
    updated = (segment_rows.astype(jnp.float32) + gate_here * summed).astype(jnp.bfloat16)
    updated = updated.reshape(frames, span, narrow)
    moved = pass_onward(relay_features(updated))
    return moved.reshape(1, 1, patches, narrow)


def solution(mesh):
    seg, seq, mp = mesh.devices.shape
    inner = mesh.devices.reshape(seg, 2, seq // 4, 2, mp)
    fine = jax.sharding.Mesh(inner, ("segment", "zh", "x", "c", "mp"))
    return jax.shard_map(
        on_device,
        mesh=fine,
        in_specs=(
            P("segment", SEQ, None, "mp"),
            P("segment", SEQ, None, "mp"),
            P("segment", "mp", SEQ),
            P("segment", None),
            P("segment", None),
            P("segment", None),
            P("segment", None),
        ),
        out_specs=P("segment", SEQ, None, "mp"),
        check_vma=False,
    )
```

```python
import math

import jax
import jax.numpy as jnp
from jax import lax
from jax.sharding import PartitionSpec as P

HD = 128


EPS = 1e-06
NEG_FILL = -1e30


def passed_along(x, axis, by):
    length = lax.axis_size(axis)
    return lax.ppermute(x, axis, [(i, (i + by) % length) for i in range(length)])


def masked_attention(queries, keys_in, values, usable):
    factor = 1.0 / math.sqrt(queries.shape[-1])
    scores = (
        jnp.einsum("...ihe,...jhe->...hij", queries, keys_in, preferred_element_type=jnp.float32)
        * factor
    )
    allowed = usable[..., None, :, None] & usable[..., None, None, :]
    masked = jnp.where(allowed, scores, NEG_FILL)
    highest = jnp.max(masked, axis=-1, keepdims=True)
    raised = jnp.where(allowed, jnp.exp(masked - highest), 0.0)
    spare_one = jnp.where(usable, 0.0, 1.0)[..., None, :, None]
    weights = (raised / (jnp.sum(raised, axis=-1, keepdims=True) + spare_one)).astype(jnp.bfloat16)
    blended = jnp.einsum(
        "...hij,...jhe->...ihe", weights, values, preferred_element_type=jnp.float32
    )
    return blended.astype(jnp.bfloat16)


SEQ = ("zh", "x", "c")


def seq_index():
    return (lax.axis_index("zh") * lax.axis_size("x") + lax.axis_index("x")) * lax.axis_size(
        "c"
    ) + lax.axis_index("c")


def swap(block, axis):
    return lax.ppermute(block, axis, [(0, 1), (1, 0)])


def spread_seq(block):
    zh = lax.axis_index("zh")
    x = lax.axis_index("x")
    c = lax.axis_index("c")
    nx = lax.axis_size("x")
    held = [(zh, x, block), (1 - zh, x, swap(block, "zh"))]
    for bz, bx, piece in list(held):
        for s in range(1, nx):
            moved = lax.ppermute(piece, "x", [(k, (k + s) % nx) for k in range(nx)])
            held.append((bz, (bx - s) % nx, moved))
    out = []
    for bz, bx, piece in held:
        out.append(((bz * nx + bx) * 2 + c, piece))
        out.append(((bz * nx + bx) * 2 + 1 - c, swap(piece, "c")))
    return out


def relay_features(rows_now):
    return lax.all_to_all(rows_now, SEQ, split_axis=0, concat_axis=0, tiled=True)


def pass_onward(rows_now):
    return passed_along(rows_now, "segment", 1)


def on_device(latents, w_qkv, w_out, mod_shift, mod_scale, mod_gate, counts):
    frames = lax.axis_size(SEQ)
    patches = latents.shape[2]
    narrow = latents.shape[3]
    span = patches // frames
    segment_rows = latents[0, 0]
    gathered = lax.all_gather(latents, "mp", axis=3, tiled=True)[0, 0]
    widened = gathered.astype(jnp.float32)
    average = jnp.mean(widened, axis=-1, keepdims=True)
    centred = widened - average
    variance = jnp.mean(centred * centred, axis=-1, keepdims=True)
    modulated = (centred * lax.rsqrt(variance + EPS) * mod_scale[0] + mod_shift[0]).astype(
        jnp.bfloat16
    )
    columns = w_qkv.shape[2] * w_qkv.shape[3]
    rows = w_qkv.shape[1]
    projected = None
    for where, piece in spread_seq(w_qkv[0].reshape(rows, columns)):
        part = jnp.dot(
            lax.dynamic_slice_in_dim(modulated, where * rows, rows, axis=1),
            piece,
            preferred_element_type=jnp.float32,
        )
        projected = part if projected is None else projected + part
    local_heads = w_qkv.shape[3] // HD
    projected = projected.astype(jnp.bfloat16).reshape(patches, 3, local_heads, HD)
    frame_here = seq_index()
    clip_counts = counts[0]
    positions = jnp.arange(frames)

    def spatial(triple):
        count_here = jnp.sum(jnp.where(positions == frame_here, clip_counts, 0))
        usable = jnp.arange(patches) < count_here
        return masked_attention(triple[:, 0], triple[:, 1], triple[:, 2], usable)

    def temporal(triple):
        by_place = triple.reshape(frames, span, 3, local_heads, HD).transpose(1, 0, 2, 3, 4)
        location = frame_here * span + jnp.arange(span)
        usable = location[:, None] < clip_counts[None, :]
        blended = masked_attention(by_place[:, :, 0], by_place[:, :, 1], by_place[:, :, 2], usable)
        return blended.transpose(1, 0, 2, 3).reshape(patches, local_heads, HD)

    attended = lax.cond(lax.axis_index("segment") % 2 == 0, spatial, temporal, projected)
    attended = attended.reshape(patches, local_heads * HD)
    member = lax.axis_index("mp")
    width = w_out.shape[2]
    partials = jnp.zeros((patches, width * frames), jnp.bfloat16)
    for where, piece in spread_seq(w_out[0]):
        part = jnp.dot(attended, piece, preferred_element_type=jnp.float32)
        partials = lax.dynamic_update_slice_in_dim(
            partials, part.astype(jnp.bfloat16), where * width, axis=1
        )
    summed = lax.psum_scatter(partials, "mp", scatter_dimension=1, tiled=True).astype(
        jnp.float32
    )
    gate_here = lax.dynamic_slice_in_dim(mod_gate[0], member * narrow, narrow)
    updated = (segment_rows.astype(jnp.float32) + gate_here * summed).astype(jnp.bfloat16)
    updated = updated.reshape(frames, span, narrow)
    moved = pass_onward(relay_features(updated))
    return moved.reshape(1, 1, patches, narrow)


def solution(mesh):
    seg, seq, mp = mesh.devices.shape
    inner = mesh.devices.reshape(seg, 2, seq // 4, 2, mp)
    fine = jax.sharding.Mesh(inner, ("segment", "zh", "x", "c", "mp"))
    return jax.shard_map(
        on_device,
        mesh=fine,
        in_specs=(
            P("segment", SEQ, None, "mp"),
            P("segment", SEQ, None, "mp"),
            P("segment", "mp", SEQ),
            P("segment", None),
            P("segment", None),
            P("segment", None),
            P("segment", None),
        ),
        out_specs=P("segment", SEQ, None, "mp"),
        check_vma=False,
    )
```

```python
import math

import jax
import jax.numpy as jnp
from jax import lax
from jax.sharding import PartitionSpec as P

HD = 128


EPS = 1e-06
NEG_FILL = -1e30


def passed_along(x, axis, by):
    length = lax.axis_size(axis)
    return lax.ppermute(x, axis, [(i, (i + by) % length) for i in range(length)])


def masked_attention(queries, keys_in, values, usable):
    factor = 1.0 / math.sqrt(queries.shape[-1])
    scores = (
        jnp.einsum("...ihe,...jhe->...hij", queries, keys_in, preferred_element_type=jnp.float32)
        * factor
    )
    allowed = usable[..., None, :, None] & usable[..., None, None, :]
    masked = jnp.where(allowed, scores, NEG_FILL)
    highest = jnp.max(masked, axis=-1, keepdims=True)
    raised = jnp.where(allowed, jnp.exp(masked - highest), 0.0)
    spare_one = jnp.where(usable, 0.0, 1.0)[..., None, :, None]
    weights = (raised / (jnp.sum(raised, axis=-1, keepdims=True) + spare_one)).astype(jnp.bfloat16)
    blended = jnp.einsum(
        "...hij,...jhe->...ihe", weights, values, preferred_element_type=jnp.float32
    )
    return blended.astype(jnp.bfloat16)


SEQ = ("zh", "x", "c")


def seq_index():
    return (lax.axis_index("zh") * lax.axis_size("x") + lax.axis_index("x")) * lax.axis_size(
        "c"
    ) + lax.axis_index("c")


def swap(block, axis):
    return lax.ppermute(block, axis, [(0, 1), (1, 0)])


def spread_seq(block):
    zh = lax.axis_index("zh")
    x = lax.axis_index("x")
    c = lax.axis_index("c")
    nx = lax.axis_size("x")
    held = [(zh, x, block), (1 - zh, x, swap(block, "zh"))]
    reached = []
    for bz, bx, piece in held:
        reached.append((bz, bx, piece))
        if nx == 4:
            ahead = lax.ppermute(piece, "x", [(k, (k + 1) % nx) for k in range(nx)])
            behind = lax.ppermute(piece, "x", [(k, (k - 1) % nx) for k in range(nx)])
            onward = jnp.where(c == 0, ahead, behind)
            pairs = [(k * 2, ((k + 1) % nx) * 2) for k in range(nx)]
            pairs += [(k * 2 + 1, ((k - 1) % nx) * 2 + 1) for k in range(nx)]
            far = lax.ppermute(onward, ("x", "c"), pairs)
            reached.append((bz, (bx - 1) % nx, ahead))
            reached.append((bz, (bx + 1) % nx, behind))
            reached.append((bz, (bx + 2) % nx, far))
        else:
            for s in range(1, nx):
                moved = lax.ppermute(piece, "x", [(k, (k + s) % nx) for k in range(nx)])
                reached.append((bz, (bx - s) % nx, moved))
    out = []
    for bz, bx, piece in reached:
        out.append(((bz * nx + bx) * 2 + c, piece))
        out.append(((bz * nx + bx) * 2 + 1 - c, swap(piece, "c")))
    return out


def relay_features(rows_now):
    return lax.all_to_all(rows_now, SEQ, split_axis=0, concat_axis=0, tiled=True)


def pass_onward(rows_now):
    return passed_along(rows_now, "segment", 1)


def on_device(latents, w_qkv, w_out, mod_shift, mod_scale, mod_gate, counts):
    frames = lax.axis_size(SEQ)
    patches = latents.shape[2]
    narrow = latents.shape[3]
    span = patches // frames
    segment_rows = latents[0, 0]
    gathered = lax.all_gather(latents, "mp", axis=3, tiled=True)[0, 0]
    widened = gathered.astype(jnp.float32)
    average = jnp.mean(widened, axis=-1, keepdims=True)
    centred = widened - average
    variance = jnp.mean(centred * centred, axis=-1, keepdims=True)
    modulated = (centred * lax.rsqrt(variance + EPS) * mod_scale[0] + mod_shift[0]).astype(
        jnp.bfloat16
    )
    columns = w_qkv.shape[2] * w_qkv.shape[3]
    rows = w_qkv.shape[1]
    payload = jnp.concatenate([w_qkv[0].reshape(rows, columns), w_out[0].T], axis=1)
    arrived = spread_seq(payload)
    sources = [where for where, _ in arrived]
    w_in = jnp.concatenate([piece[:, :columns] for _, piece in arrived], axis=0)
    reordered = jnp.concatenate(
        [lax.dynamic_slice_in_dim(modulated, where * rows, rows, axis=1) for where in sources],
        axis=1,
    )
    projected = jnp.dot(reordered, w_in, preferred_element_type=jnp.float32)
    local_heads = w_qkv.shape[3] // HD
    projected = projected.astype(jnp.bfloat16).reshape(patches, 3, local_heads, HD)
    frame_here = seq_index()
    clip_counts = counts[0]
    positions = jnp.arange(frames)

    def spatial(triple):
        count_here = jnp.sum(jnp.where(positions == frame_here, clip_counts, 0))
        usable = jnp.arange(patches) < count_here
        return masked_attention(triple[:, 0], triple[:, 1], triple[:, 2], usable)

    def temporal(triple):
        by_place = triple.reshape(frames, span, 3, local_heads, HD).transpose(1, 0, 2, 3, 4)
        location = frame_here * span + jnp.arange(span)
        usable = location[:, None] < clip_counts[None, :]
        blended = masked_attention(by_place[:, :, 0], by_place[:, :, 1], by_place[:, :, 2], usable)
        return blended.transpose(1, 0, 2, 3).reshape(patches, local_heads, HD)

    attended = lax.cond(lax.axis_index("segment") % 2 == 0, spatial, temporal, projected)
    attended = attended.reshape(patches, local_heads * HD)
    member = lax.axis_index("mp")
    width = w_out.shape[2]
    w_back = jnp.concatenate([piece[:, columns:] for _, piece in arrived], axis=0)
    mixed = jnp.einsum(
        "tr,cr->tc", attended, w_back, preferred_element_type=jnp.float32
    ).astype(jnp.bfloat16)
    partials = jnp.zeros((patches, width * frames), jnp.bfloat16)
    for slot, where in enumerate(sources):
        partials = lax.dynamic_update_slice_in_dim(
            partials, mixed[:, slot * width : (slot + 1) * width], where * width, axis=1
        )
    summed = lax.psum_scatter(partials, "mp", scatter_dimension=1, tiled=True).astype(
        jnp.float32
    )
    gate_here = lax.dynamic_slice_in_dim(mod_gate[0], member * narrow, narrow)
    updated = (segment_rows.astype(jnp.float32) + gate_here * summed).astype(jnp.bfloat16)
    updated = updated.reshape(frames, span, narrow)
    moved = pass_onward(relay_features(updated))
    return moved.reshape(1, 1, patches, narrow)


def solution(mesh):
    seg, seq, mp = mesh.devices.shape
    inner = mesh.devices.reshape(seg, 2, seq // 4, 2, mp)
    fine = jax.sharding.Mesh(inner, ("segment", "zh", "x", "c", "mp"))
    return jax.shard_map(
        on_device,
        mesh=fine,
        in_specs=(
            P("segment", SEQ, None, "mp"),
            P("segment", SEQ, None, "mp"),
            P("segment", "mp", SEQ),
            P("segment", None),
            P("segment", None),
            P("segment", None),
            P("segment", None),
        ),
        out_specs=P("segment", SEQ, None, "mp"),
        check_vma=False,
    )
```

```python
import math

import jax
import jax.numpy as jnp
from jax import lax
from jax.sharding import PartitionSpec as P

HD = 128


EPS = 1e-06
NEG_FILL = -1e30


def passed_along(x, axis, by):
    length = lax.axis_size(axis)
    return lax.ppermute(x, axis, [(i, (i + by) % length) for i in range(length)])


def masked_attention(queries, keys_in, values, usable):
    factor = 1.0 / math.sqrt(queries.shape[-1])
    scores = (
        jnp.einsum("...ihe,...jhe->...hij", queries, keys_in, preferred_element_type=jnp.float32)
        * factor
    )
    allowed = usable[..., None, :, None] & usable[..., None, None, :]
    masked = jnp.where(allowed, scores, NEG_FILL)
    highest = jnp.max(masked, axis=-1, keepdims=True)
    raised = jnp.where(allowed, jnp.exp(masked - highest), 0.0)
    spare_one = jnp.where(usable, 0.0, 1.0)[..., None, :, None]
    weights = (raised / (jnp.sum(raised, axis=-1, keepdims=True) + spare_one)).astype(jnp.bfloat16)
    blended = jnp.einsum(
        "...hij,...jhe->...ihe", weights, values, preferred_element_type=jnp.float32
    )
    return blended.astype(jnp.bfloat16)


SEQ = ("zh", "x", "c")


def seq_index():
    return (lax.axis_index("zh") * lax.axis_size("x") + lax.axis_index("x")) * lax.axis_size(
        "c"
    ) + lax.axis_index("c")


def swap(block, axis):
    return lax.ppermute(block, axis, [(0, 1), (1, 0)])


def spread_seq(block):
    zh = lax.axis_index("zh")
    x = lax.axis_index("x")
    c = lax.axis_index("c")
    nx = lax.axis_size("x")
    held = [(zh, x, block), (1 - zh, x, swap(block, "zh"))]
    reached = []
    for bz, bx, piece in held:
        reached.append((bz, bx, piece))
        if nx == 4:
            ahead = lax.ppermute(piece, "x", [(k, (k + 1) % nx) for k in range(nx)])
            behind = lax.ppermute(piece, "x", [(k, (k - 1) % nx) for k in range(nx)])
            onward = jnp.where(c == 0, ahead, behind)
            pairs = [(k * 2, ((k + 1) % nx) * 2) for k in range(nx)]
            pairs += [(k * 2 + 1, ((k - 1) % nx) * 2 + 1) for k in range(nx)]
            far = lax.ppermute(onward, ("x", "c"), pairs)
            reached.append((bz, (bx - 1) % nx, ahead))
            reached.append((bz, (bx + 1) % nx, behind))
            reached.append((bz, (bx + 2) % nx, far))
        else:
            for s in range(1, nx):
                moved = lax.ppermute(piece, "x", [(k, (k + s) % nx) for k in range(nx)])
                reached.append((bz, (bx - s) % nx, moved))
    return [(bz * nx + bx, piece) for bz, bx, piece in reached]


def relay_features(rows_now):
    return lax.all_to_all(rows_now, SEQ, split_axis=0, concat_axis=0, tiled=True)


def pass_onward(rows_now):
    return passed_along(rows_now, "segment", 1)


def on_device(latents, w_qkv, w_out, mod_shift, mod_scale, mod_gate, counts):
    frames = lax.axis_size(SEQ)
    patches = latents.shape[2]
    narrow = latents.shape[3]
    span = patches // frames
    segment_rows = latents[0, 0]
    gathered = lax.all_gather(latents, "mp", axis=3, tiled=True)[0, 0]
    widened = gathered.astype(jnp.float32)
    average = jnp.mean(widened, axis=-1, keepdims=True)
    centred = widened - average
    variance = jnp.mean(centred * centred, axis=-1, keepdims=True)
    modulated = (centred * lax.rsqrt(variance + EPS) * mod_scale[0] + mod_shift[0]).astype(
        jnp.bfloat16
    )
    columns = w_qkv.shape[2] * w_qkv.shape[3]
    rows = w_qkv.shape[1]
    payload = jnp.concatenate([w_qkv[0].reshape(rows, columns), w_out[0].T], axis=1)
    arrived = spread_seq(payload)
    core = lax.axis_index("c")
    pair_rows = jnp.concatenate([modulated, swap(modulated, "c")], axis=0)
    w_in = jnp.concatenate([piece[:, :columns] for _, piece in arrived], axis=0)
    reordered = jnp.concatenate(
        [
            lax.dynamic_slice_in_dim(pair_rows, (chip * 2 + core) * rows, rows, axis=1)
            for chip, _ in arrived
        ],
        axis=1,
    )
    both = jnp.dot(reordered, w_in, preferred_element_type=jnp.float32)
    projected = both[:patches] + swap(both[patches:], "c")
    local_heads = w_qkv.shape[3] // HD
    projected = projected.astype(jnp.bfloat16).reshape(patches, 3, local_heads, HD)
    frame_here = seq_index()
    clip_counts = counts[0]
    positions = jnp.arange(frames)

    def spatial(triple):
        count_here = jnp.sum(jnp.where(positions == frame_here, clip_counts, 0))
        usable = jnp.arange(patches) < count_here
        return masked_attention(triple[:, 0], triple[:, 1], triple[:, 2], usable)

    def temporal(triple):
        by_place = triple.reshape(frames, span, 3, local_heads, HD).transpose(1, 0, 2, 3, 4)
        location = frame_here * span + jnp.arange(span)
        usable = location[:, None] < clip_counts[None, :]
        blended = masked_attention(by_place[:, :, 0], by_place[:, :, 1], by_place[:, :, 2], usable)
        return blended.transpose(1, 0, 2, 3).reshape(patches, local_heads, HD)

    attended = lax.cond(lax.axis_index("segment") % 2 == 0, spatial, temporal, projected)
    attended = attended.reshape(patches, local_heads * HD)
    member = lax.axis_index("mp")
    width = w_out.shape[2]
    pair_att = jnp.concatenate([attended, swap(attended, "c")], axis=0)
    w_back = jnp.concatenate([piece[:, columns:] for _, piece in arrived], axis=0)
    mixed = jnp.einsum(
        "tr,cr->tc", pair_att, w_back, preferred_element_type=jnp.float32
    ).astype(jnp.bfloat16)
    partials = jnp.zeros((2 * patches, width * frames // 2), jnp.bfloat16)
    for slot, (chip, _) in enumerate(arrived):
        partials = lax.dynamic_update_slice_in_dim(
            partials, mixed[:, slot * width : (slot + 1) * width], chip * width, axis=1
        )
    pair_sum = lax.psum_scatter(partials, "mp", scatter_dimension=1, tiled=True)
    mine = pair_sum[:patches]
    theirs = swap(pair_sum[patches:], "c")
    summed = jnp.where(
        core == 0,
        jnp.concatenate([mine, theirs], axis=1),
        jnp.concatenate([theirs, mine], axis=1),
    ).astype(jnp.float32)
    gate_here = lax.dynamic_slice_in_dim(mod_gate[0], member * narrow, narrow)
    updated = (segment_rows.astype(jnp.float32) + gate_here * summed).astype(jnp.bfloat16)
    updated = updated.reshape(frames, span, narrow)
    moved = pass_onward(relay_features(updated))
    return moved.reshape(1, 1, patches, narrow)


def solution(mesh):
    seg, seq, mp = mesh.devices.shape
    inner = mesh.devices.reshape(seg, 2, seq // 4, 2, mp)
    fine = jax.sharding.Mesh(inner, ("segment", "zh", "x", "c", "mp"))
    return jax.shard_map(
        on_device,
        mesh=fine,
        in_specs=(
            P("segment", SEQ, None, "mp"),
            P("segment", SEQ, None, "mp"),
            P("segment", "mp", SEQ),
            P("segment", None),
            P("segment", None),
            P("segment", None),
            P("segment", None),
        ),
        out_specs=P("segment", SEQ, None, "mp"),
        check_vma=False,
    )
```

```python
import math

import jax
import jax.numpy as jnp
from jax import lax
from jax.sharding import PartitionSpec as P

HD = 128


EPS = 1e-06
NEG_FILL = -1e30


def passed_along(x, axis, by):
    length = lax.axis_size(axis)
    return lax.ppermute(x, axis, [(i, (i + by) % length) for i in range(length)])


def masked_attention(queries, keys_in, values, usable):
    factor = 1.0 / math.sqrt(queries.shape[-1])
    scores = (
        jnp.einsum("...ihe,...jhe->...hij", queries, keys_in, preferred_element_type=jnp.float32)
        * factor
    )
    allowed = usable[..., None, :, None] & usable[..., None, None, :]
    masked = jnp.where(allowed, scores, NEG_FILL)
    highest = jnp.max(masked, axis=-1, keepdims=True)
    raised = jnp.where(allowed, jnp.exp(masked - highest), 0.0)
    spare_one = jnp.where(usable, 0.0, 1.0)[..., None, :, None]
    weights = (raised / (jnp.sum(raised, axis=-1, keepdims=True) + spare_one)).astype(jnp.bfloat16)
    blended = jnp.einsum(
        "...hij,...jhe->...ihe", weights, values, preferred_element_type=jnp.float32
    )
    return blended.astype(jnp.bfloat16)


SEQ = ("zh", "x", "c")


def seq_index():
    return (lax.axis_index("zh") * lax.axis_size("x") + lax.axis_index("x")) * lax.axis_size(
        "c"
    ) + lax.axis_index("c")


def swap(block, axis):
    return lax.ppermute(block, axis, [(0, 1), (1, 0)])


def spread_seq(block, z_chunks=2):
    zh = lax.axis_index("zh")
    x = lax.axis_index("x")
    c = lax.axis_index("c")
    nx = lax.axis_size("x")
    step = block.shape[0] // z_chunks
    held = [(zh, x, 0, block)]
    for k in range(z_chunks):
        held.append((1 - zh, x, k * step, swap(block[k * step : (k + 1) * step], "zh")))
    reached = []
    for bz, bx, first, piece in held:
        reached.append((bz, bx, first, piece))
        if nx == 4:
            ahead = lax.ppermute(piece, "x", [(k, (k + 1) % nx) for k in range(nx)])
            behind = lax.ppermute(piece, "x", [(k, (k - 1) % nx) for k in range(nx)])
            onward = jnp.where(c == 0, ahead, behind)
            pairs = [(k * 2, ((k + 1) % nx) * 2) for k in range(nx)]
            pairs += [(k * 2 + 1, ((k - 1) % nx) * 2 + 1) for k in range(nx)]
            far = lax.ppermute(onward, ("x", "c"), pairs)
            reached.append((bz, (bx - 1) % nx, first, ahead))
            reached.append((bz, (bx + 1) % nx, first, behind))
            reached.append((bz, (bx + 2) % nx, first, far))
        else:
            for s in range(1, nx):
                moved = lax.ppermute(piece, "x", [(k, (k + s) % nx) for k in range(nx)])
                reached.append((bz, (bx - s) % nx, first, moved))
    return [(bz * nx + bx, first, piece) for bz, bx, first, piece in reached]


def relay_features(rows_now):
    return lax.all_to_all(rows_now, SEQ, split_axis=0, concat_axis=0, tiled=True)


def pass_onward(rows_now):
    return passed_along(rows_now, "segment", 1)


def on_device(latents, w_qkv, w_out, mod_shift, mod_scale, mod_gate, counts):
    frames = lax.axis_size(SEQ)
    patches = latents.shape[2]
    narrow = latents.shape[3]
    span = patches // frames
    segment_rows = latents[0, 0]
    gathered = lax.all_gather(latents, "mp", axis=3, tiled=True)[0, 0]
    widened = gathered.astype(jnp.float32)
    average = jnp.mean(widened, axis=-1, keepdims=True)
    centred = widened - average
    variance = jnp.mean(centred * centred, axis=-1, keepdims=True)
    modulated = (centred * lax.rsqrt(variance + EPS) * mod_scale[0] + mod_shift[0]).astype(
        jnp.bfloat16
    )
    columns = w_qkv.shape[2] * w_qkv.shape[3]
    rows = w_qkv.shape[1]
    payload = jnp.concatenate([w_qkv[0].reshape(rows, columns), w_out[0].T], axis=1)
    arrived = spread_seq(payload)
    core = lax.axis_index("c")
    pair_rows = jnp.concatenate([modulated, swap(modulated, "c")], axis=0)
    w_in = jnp.concatenate([piece[:, :columns] for _, _, piece in arrived], axis=0)
    reordered = jnp.concatenate(
        [
            lax.dynamic_slice_in_dim(
                pair_rows, (chip * 2 + core) * rows + first, piece.shape[0], axis=1
            )
            for chip, first, piece in arrived
        ],
        axis=1,
    )
    both = jnp.dot(reordered, w_in, preferred_element_type=jnp.float32)
    projected = both[:patches] + swap(both[patches:], "c")
    local_heads = w_qkv.shape[3] // HD
    projected = projected.astype(jnp.bfloat16).reshape(patches, 3, local_heads, HD)
    frame_here = seq_index()
    clip_counts = counts[0]
    positions = jnp.arange(frames)

    def spatial(triple):
        count_here = jnp.sum(jnp.where(positions == frame_here, clip_counts, 0))
        usable = jnp.arange(patches) < count_here
        return masked_attention(triple[:, 0], triple[:, 1], triple[:, 2], usable)

    def temporal(triple):
        by_place = triple.reshape(frames, span, 3, local_heads, HD).transpose(1, 0, 2, 3, 4)
        location = frame_here * span + jnp.arange(span)
        usable = location[:, None] < clip_counts[None, :]
        blended = masked_attention(by_place[:, :, 0], by_place[:, :, 1], by_place[:, :, 2], usable)
        return blended.transpose(1, 0, 2, 3).reshape(patches, local_heads, HD)

    attended = lax.cond(lax.axis_index("segment") % 2 == 0, spatial, temporal, projected)
    attended = attended.reshape(patches, local_heads * HD)
    member = lax.axis_index("mp")
    width = w_out.shape[2]
    pair_att = jnp.concatenate([attended, swap(attended, "c")], axis=0)
    w_back = jnp.concatenate([piece[:, columns:] for _, _, piece in arrived], axis=0)
    mixed = jnp.einsum(
        "tr,cr->tc", pair_att, w_back, preferred_element_type=jnp.float32
    ).astype(jnp.bfloat16)
    partials = jnp.zeros((2 * patches, width * frames // 2), jnp.bfloat16)
    slot = 0
    for chip, first, piece in arrived:
        size = piece.shape[0]
        partials = lax.dynamic_update_slice_in_dim(
            partials, mixed[:, slot : slot + size], chip * width + first, axis=1
        )
        slot += size
    pair_sum = lax.psum_scatter(partials, "mp", scatter_dimension=1, tiled=True)
    mine = pair_sum[:patches]
    theirs = swap(pair_sum[patches:], "c")
    summed = jnp.where(
        core == 0,
        jnp.concatenate([mine, theirs], axis=1),
        jnp.concatenate([theirs, mine], axis=1),
    ).astype(jnp.float32)
    gate_here = lax.dynamic_slice_in_dim(mod_gate[0], member * narrow, narrow)
    updated = (segment_rows.astype(jnp.float32) + gate_here * summed).astype(jnp.bfloat16)
    updated = updated.reshape(frames, span, narrow)
    moved = pass_onward(relay_features(updated))
    return moved.reshape(1, 1, patches, narrow)


def solution(mesh):
    seg, seq, mp = mesh.devices.shape
    inner = mesh.devices.reshape(seg, 2, seq // 4, 2, mp)
    fine = jax.sharding.Mesh(inner, ("segment", "zh", "x", "c", "mp"))
    return jax.shard_map(
        on_device,
        mesh=fine,
        in_specs=(
            P("segment", SEQ, None, "mp"),
            P("segment", SEQ, None, "mp"),
            P("segment", "mp", SEQ),
            P("segment", None),
            P("segment", None),
            P("segment", None),
            P("segment", None),
        ),
        out_specs=P("segment", SEQ, None, "mp"),
        check_vma=False,
    )
```

```python
import math

import jax
import jax.numpy as jnp
from jax import lax
from jax.sharding import PartitionSpec as P

HD = 128


EPS = 1e-06
NEG_FILL = -1e30


def passed_along(x, axis, by):
    length = lax.axis_size(axis)
    return lax.ppermute(x, axis, [(i, (i + by) % length) for i in range(length)])


def masked_attention(queries, keys_in, values, usable):
    factor = 1.0 / math.sqrt(queries.shape[-1])
    scores = (
        jnp.einsum("...ihe,...jhe->...hij", queries, keys_in, preferred_element_type=jnp.float32)
        * factor
    )
    allowed = usable[..., None, :, None] & usable[..., None, None, :]
    masked = jnp.where(allowed, scores, NEG_FILL)
    highest = jnp.max(masked, axis=-1, keepdims=True)
    raised = jnp.where(allowed, jnp.exp(masked - highest), 0.0)
    spare_one = jnp.where(usable, 0.0, 1.0)[..., None, :, None]
    weights = (raised / (jnp.sum(raised, axis=-1, keepdims=True) + spare_one)).astype(jnp.bfloat16)
    blended = jnp.einsum(
        "...hij,...jhe->...ihe", weights, values, preferred_element_type=jnp.float32
    )
    return blended.astype(jnp.bfloat16)


SEQ = ("zh", "x", "c")


def seq_index():
    return (lax.axis_index("zh") * lax.axis_size("x") + lax.axis_index("x")) * lax.axis_size(
        "c"
    ) + lax.axis_index("c")


def swap(block, axis):
    return lax.ppermute(block, axis, [(0, 1), (1, 0)])


def spread_seq(block):
    zh = lax.axis_index("zh")
    x = lax.axis_index("x")
    c = lax.axis_index("c")
    nx = lax.axis_size("x")
    held = [(zh, x, block), (1 - zh, x, swap(block, "zh"))]
    reached = []
    for bz, bx, piece in held:
        reached.append((bz, bx, piece))
        if nx == 4:
            ahead = lax.ppermute(piece, "x", [(k, (k + 1) % nx) for k in range(nx)])
            behind = lax.ppermute(piece, "x", [(k, (k - 1) % nx) for k in range(nx)])
            onward = jnp.where(c == 0, ahead, behind)
            pairs = [(k * 2, ((k + 1) % nx) * 2) for k in range(nx)]
            pairs += [(k * 2 + 1, ((k - 1) % nx) * 2 + 1) for k in range(nx)]
            far = lax.ppermute(onward, ("x", "c"), pairs)
            reached.append((bz, (bx - 1) % nx, ahead))
            reached.append((bz, (bx + 1) % nx, behind))
            reached.append((bz, (bx + 2) % nx, far))
        else:
            for s in range(1, nx):
                moved = lax.ppermute(piece, "x", [(k, (k + s) % nx) for k in range(nx)])
                reached.append((bz, (bx - s) % nx, moved))
    return [(bz * nx + bx, piece) for bz, bx, piece in reached]


def relay_onward(rows_now):
    halves = lax.axis_size("zh")
    sections = lax.axis_size("segment")
    zh = lax.axis_index("zh")
    split = rows_now.reshape((halves, -1) + rows_now.shape[1:])
    local = lax.all_to_all(split, ("x", "c"), split_axis=1, concat_axis=1, tiled=True)
    stay = jnp.where(zh == 0, local[0], local[1])
    cross = jnp.where(zh == 0, local[1], local[0])
    to = lambda s, h: s * halves + h
    stay = lax.ppermute(
        stay,
        ("segment", "zh"),
        [(to(s, h), to((s + 1) % sections, h)) for s in range(sections) for h in range(halves)],
    )
    cross = lax.ppermute(
        cross,
        ("segment", "zh"),
        [(to(s, h), to((s + 1) % sections, 1 - h)) for s in range(sections) for h in range(halves)],
    )
    return jnp.where(
        zh == 0, jnp.concatenate([stay, cross], axis=0), jnp.concatenate([cross, stay], axis=0)
    )


def on_device(latents, w_qkv, w_out, mod_shift, mod_scale, mod_gate, counts):
    frames = lax.axis_size(SEQ)
    patches = latents.shape[2]
    narrow = latents.shape[3]
    span = patches // frames
    segment_rows = latents[0, 0]
    gathered = lax.all_gather(latents, "mp", axis=3, tiled=True)[0, 0]
    widened = gathered.astype(jnp.float32)
    average = jnp.mean(widened, axis=-1, keepdims=True)
    centred = widened - average
    variance = jnp.mean(centred * centred, axis=-1, keepdims=True)
    modulated = (centred * lax.rsqrt(variance + EPS) * mod_scale[0] + mod_shift[0]).astype(
        jnp.bfloat16
    )
    columns = w_qkv.shape[2] * w_qkv.shape[3]
    rows = w_qkv.shape[1]
    payload = jnp.concatenate([w_qkv[0].reshape(rows, columns), w_out[0].T], axis=1)
    arrived = spread_seq(payload)
    core = lax.axis_index("c")
    pair_rows = jnp.concatenate([modulated, swap(modulated, "c")], axis=0)
    w_in = jnp.concatenate([piece[:, :columns] for _, piece in arrived], axis=0)
    reordered = jnp.concatenate(
        [
            lax.dynamic_slice_in_dim(pair_rows, (chip * 2 + core) * rows, rows, axis=1)
            for chip, _ in arrived
        ],
        axis=1,
    )
    both = jnp.dot(reordered, w_in, preferred_element_type=jnp.float32)
    projected = both[:patches] + swap(both[patches:], "c")
    local_heads = w_qkv.shape[3] // HD
    projected = projected.astype(jnp.bfloat16).reshape(patches, 3, local_heads, HD)
    frame_here = seq_index()
    clip_counts = counts[0]
    positions = jnp.arange(frames)

    def spatial(triple):
        count_here = jnp.sum(jnp.where(positions == frame_here, clip_counts, 0))
        usable = jnp.arange(patches) < count_here
        return masked_attention(triple[:, 0], triple[:, 1], triple[:, 2], usable)

    def temporal(triple):
        by_place = triple.reshape(frames, span, 3, local_heads, HD).transpose(1, 0, 2, 3, 4)
        location = frame_here * span + jnp.arange(span)
        usable = location[:, None] < clip_counts[None, :]
        blended = masked_attention(by_place[:, :, 0], by_place[:, :, 1], by_place[:, :, 2], usable)
        return blended.transpose(1, 0, 2, 3).reshape(patches, local_heads, HD)

    attended = lax.cond(lax.axis_index("segment") % 2 == 0, spatial, temporal, projected)
    attended = attended.reshape(patches, local_heads * HD)
    member = lax.axis_index("mp")
    width = w_out.shape[2]
    pair_att = jnp.concatenate([attended, swap(attended, "c")], axis=0)
    w_back = jnp.concatenate([piece[:, columns:] for _, piece in arrived], axis=0)
    mixed = jnp.einsum(
        "tr,cr->tc", pair_att, w_back, preferred_element_type=jnp.float32
    ).astype(jnp.bfloat16)
    partials = jnp.zeros((2 * patches, width * frames // 2), jnp.bfloat16)
    for slot, (chip, _) in enumerate(arrived):
        partials = lax.dynamic_update_slice_in_dim(
            partials, mixed[:, slot * width : (slot + 1) * width], chip * width, axis=1
        )
    pair_sum = lax.psum_scatter(partials, "mp", scatter_dimension=1, tiled=True)
    mine = pair_sum[:patches]
    theirs = swap(pair_sum[patches:], "c")
    summed = jnp.where(
        core == 0,
        jnp.concatenate([mine, theirs], axis=1),
        jnp.concatenate([theirs, mine], axis=1),
    ).astype(jnp.float32)
    gate_here = lax.dynamic_slice_in_dim(mod_gate[0], member * narrow, narrow)
    updated = (segment_rows.astype(jnp.float32) + gate_here * summed).astype(jnp.bfloat16)
    updated = updated.reshape(frames, span, narrow)
    moved = relay_onward(updated)
    return moved.reshape(1, 1, patches, narrow)


def solution(mesh):
    seg, seq, mp = mesh.devices.shape
    inner = mesh.devices.reshape(seg, 2, seq // 4, 2, mp)
    fine = jax.sharding.Mesh(inner, ("segment", "zh", "x", "c", "mp"))
    return jax.shard_map(
        on_device,
        mesh=fine,
        in_specs=(
            P("segment", SEQ, None, "mp"),
            P("segment", SEQ, None, "mp"),
            P("segment", "mp", SEQ),
            P("segment", None),
            P("segment", None),
            P("segment", None),
            P("segment", None),
        ),
        out_specs=P("segment", SEQ, None, "mp"),
        check_vma=False,
    )
```

```python
import math

import jax
import jax.numpy as jnp
from jax import lax
from jax.sharding import PartitionSpec as P

HD = 128


EPS = 1e-06
NEG_FILL = -1e30


def passed_along(x, axis, by):
    length = lax.axis_size(axis)
    return lax.ppermute(x, axis, [(i, (i + by) % length) for i in range(length)])


def masked_attention(queries, keys_in, values, usable):
    factor = 1.0 / math.sqrt(queries.shape[-1])
    scores = (
        jnp.einsum("...ihe,...jhe->...hij", queries, keys_in, preferred_element_type=jnp.float32)
        * factor
    )
    allowed = usable[..., None, :, None] & usable[..., None, None, :]
    masked = jnp.where(allowed, scores, NEG_FILL)
    highest = jnp.max(masked, axis=-1, keepdims=True)
    raised = jnp.where(allowed, jnp.exp(masked - highest), 0.0)
    spare_one = jnp.where(usable, 0.0, 1.0)[..., None, :, None]
    weights = (raised / (jnp.sum(raised, axis=-1, keepdims=True) + spare_one)).astype(jnp.bfloat16)
    blended = jnp.einsum(
        "...hij,...jhe->...ihe", weights, values, preferred_element_type=jnp.float32
    )
    return blended.astype(jnp.bfloat16)


SEQ = ("zh", "x", "c")


def seq_index():
    return (lax.axis_index("zh") * lax.axis_size("x") + lax.axis_index("x")) * lax.axis_size(
        "c"
    ) + lax.axis_index("c")


def swap(block, axis):
    return lax.ppermute(block, axis, [(0, 1), (1, 0)])


def spread_seq(block):
    zh = lax.axis_index("zh")
    x = lax.axis_index("x")
    c = lax.axis_index("c")
    nx = lax.axis_size("x")
    held = [(zh, x, block), (1 - zh, x, swap(block, "zh"))]
    reached = []
    for bz, bx, piece in held:
        reached.append((bz, bx, piece))
        if nx == 4:
            ahead = lax.ppermute(piece, "x", [(k, (k + 1) % nx) for k in range(nx)])
            behind = lax.ppermute(piece, "x", [(k, (k - 1) % nx) for k in range(nx)])
            onward = jnp.where(c == 0, ahead, behind)
            pairs = [(k * 2, ((k + 1) % nx) * 2) for k in range(nx)]
            pairs += [(k * 2 + 1, ((k - 1) % nx) * 2 + 1) for k in range(nx)]
            far = lax.ppermute(onward, ("x", "c"), pairs)
            reached.append((bz, (bx - 1) % nx, ahead))
            reached.append((bz, (bx + 1) % nx, behind))
            reached.append((bz, (bx + 2) % nx, far))
        else:
            for s in range(1, nx):
                moved = lax.ppermute(piece, "x", [(k, (k + s) % nx) for k in range(nx)])
                reached.append((bz, (bx - s) % nx, moved))
    return [(bz * nx + bx, piece) for bz, bx, piece in reached]


def relay_onward(rows_now):
    halves = lax.axis_size("zh")
    sections = lax.axis_size("segment")
    zh = lax.axis_index("zh")
    split = rows_now.reshape((halves, -1) + rows_now.shape[1:])
    local = lax.all_to_all(split, ("x", "c"), split_axis=1, concat_axis=1, tiled=True)
    stay = jnp.where(zh == 0, local[0], local[1])
    cross = jnp.where(zh == 0, local[1], local[0])
    to = lambda s, h: s * halves + h
    stay = lax.ppermute(
        stay,
        ("segment", "zh"),
        [(to(s, h), to((s + 1) % sections, h)) for s in range(sections) for h in range(halves)],
    )
    cross = lax.ppermute(
        cross,
        ("segment", "zh"),
        [(to(s, h), to((s + 1) % sections, 1 - h)) for s in range(sections) for h in range(halves)],
    )
    return jnp.where(
        zh == 0, jnp.concatenate([stay, cross], axis=0), jnp.concatenate([cross, stay], axis=0)
    )


def on_device(latents, w_qkv, w_out, mod_shift, mod_scale, mod_gate, counts):
    frames = lax.axis_size(SEQ)
    patches = latents.shape[2]
    narrow = latents.shape[3]
    span = patches // frames
    segment_rows = latents[0, 0]
    gathered = lax.all_gather(latents, "mp", axis=3, tiled=True)[0, 0]
    widened = gathered.astype(jnp.float32)
    average = jnp.mean(widened, axis=-1, keepdims=True)
    centred = widened - average
    variance = jnp.mean(centred * centred, axis=-1, keepdims=True)
    modulated = (centred * lax.rsqrt(variance + EPS) * mod_scale[0] + mod_shift[0]).astype(
        jnp.bfloat16
    )
    columns = w_qkv.shape[2] * w_qkv.shape[3]
    rows = w_qkv.shape[1]
    payload = jnp.concatenate([w_qkv[0].reshape(rows, columns), w_out[0].T], axis=1)
    arrived = spread_seq(payload)
    core = lax.axis_index("c")
    pair_rows = jnp.concatenate([modulated, swap(modulated, "c")], axis=0)
    w_in = jnp.concatenate([piece[:, :columns] for _, piece in arrived], axis=0)
    reordered = jnp.concatenate(
        [
            lax.dynamic_slice_in_dim(pair_rows, (chip * 2 + core) * rows, rows, axis=1)
            for chip, _ in arrived
        ],
        axis=1,
    )
    both = jnp.dot(reordered, w_in, preferred_element_type=jnp.float32)
    projected = both[:patches] + swap(both[patches:], "c")
    local_heads = w_qkv.shape[3] // HD
    projected = projected.astype(jnp.bfloat16).reshape(patches, 3, local_heads, HD)
    frame_here = seq_index()
    clip_counts = counts[0]
    positions = jnp.arange(frames)

    def spatial(triple):
        count_here = jnp.sum(jnp.where(positions == frame_here, clip_counts, 0))
        usable = jnp.arange(patches) < count_here
        return masked_attention(triple[:, 0], triple[:, 1], triple[:, 2], usable)

    def temporal(triple):
        by_place = triple.reshape(frames, span, 3, local_heads, HD).transpose(1, 0, 2, 3, 4)
        location = frame_here * span + jnp.arange(span)
        usable = location[:, None] < clip_counts[None, :]
        blended = masked_attention(by_place[:, :, 0], by_place[:, :, 1], by_place[:, :, 2], usable)
        return blended.transpose(1, 0, 2, 3).reshape(patches, local_heads, HD)

    attended = lax.cond(lax.axis_index("segment") % 2 == 0, spatial, temporal, projected)
    attended = attended.reshape(patches, local_heads * HD)
    member = lax.axis_index("mp")
    width = w_out.shape[2]
    pair_att = jnp.concatenate([attended, swap(attended, "c")], axis=0)
    w_back = jnp.concatenate([piece[:, columns:] for _, piece in arrived], axis=0)
    mixed = jnp.einsum(
        "tr,cr->tc", pair_att, w_back, preferred_element_type=jnp.float32
    ).astype(jnp.bfloat16)
    partials = jnp.zeros((2 * patches, width * frames // 2), jnp.bfloat16)
    for slot, (chip, _) in enumerate(arrived):
        partials = lax.dynamic_update_slice_in_dim(
            partials, mixed[:, slot * width : (slot + 1) * width], chip * width, axis=1
        )
    mine = lax.psum_scatter(partials[:patches], "mp", scatter_dimension=1, tiled=True)
    groups = lax.axis_size("mp")
    spread = partials[patches:].reshape(patches, groups, -1)
    gathered_parts = lax.all_to_all(spread, "mp", split_axis=1, concat_axis=1, tiled=True)
    other = jnp.sum(gathered_parts.astype(jnp.float32), axis=1).astype(jnp.bfloat16)
    theirs = swap(other, "c")
    summed = jnp.where(
        core == 0,
        jnp.concatenate([mine, theirs], axis=1),
        jnp.concatenate([theirs, mine], axis=1),
    ).astype(jnp.float32)
    gate_here = lax.dynamic_slice_in_dim(mod_gate[0], member * narrow, narrow)
    updated = (segment_rows.astype(jnp.float32) + gate_here * summed).astype(jnp.bfloat16)
    updated = updated.reshape(frames, span, narrow)
    moved = relay_onward(updated)
    return moved.reshape(1, 1, patches, narrow)


def solution(mesh):
    seg, seq, mp = mesh.devices.shape
    inner = mesh.devices.reshape(seg, 2, seq // 4, 2, mp)
    fine = jax.sharding.Mesh(inner, ("segment", "zh", "x", "c", "mp"))
    return jax.shard_map(
        on_device,
        mesh=fine,
        in_specs=(
            P("segment", SEQ, None, "mp"),
            P("segment", SEQ, None, "mp"),
            P("segment", "mp", SEQ),
            P("segment", None),
            P("segment", None),
            P("segment", None),
            P("segment", None),
        ),
        out_specs=P("segment", SEQ, None, "mp"),
        check_vma=False,
    )
```

```python
import math

import jax
import jax.numpy as jnp
from jax import lax
from jax.sharding import PartitionSpec as P


HD = 128


EPS = 1e-06
NEG_FILL = -1e30


def masked_attention(queries, keys_in, values, usable):
    factor = 1.0 / math.sqrt(queries.shape[-1])
    scores = (
        jnp.einsum("...ihe,...jhe->...hij", queries, keys_in, preferred_element_type=jnp.float32)
        * factor
    )
    allowed = usable[..., None, :, None] & usable[..., None, None, :]
    masked = jnp.where(allowed, scores, NEG_FILL)
    highest = jnp.max(masked, axis=-1, keepdims=True)
    raised = jnp.where(allowed, jnp.exp(masked - highest), 0.0)
    spare_one = jnp.where(usable, 0.0, 1.0)[..., None, :, None]
    weights = (raised / (jnp.sum(raised, axis=-1, keepdims=True) + spare_one)).astype(jnp.bfloat16)
    blended = jnp.einsum(
        "...hij,...jhe->...ihe", weights, values, preferred_element_type=jnp.float32
    )
    return blended.astype(jnp.bfloat16)


SEQ = ("zh", "x", "c")


def seq_index():
    return (lax.axis_index("zh") * lax.axis_size("x") + lax.axis_index("x")) * lax.axis_size(
        "c"
    ) + lax.axis_index("c")


def swap(block, axis):
    return lax.ppermute(block, axis, [(0, 1), (1, 0)])


def spread_seq(block):
    zh = lax.axis_index("zh")
    x = lax.axis_index("x")
    c = lax.axis_index("c")
    nx = lax.axis_size("x")
    held = [(zh, x, block), (1 - zh, x, swap(block, "zh"))]
    reached = []
    for bz, bx, piece in held:
        reached.append((bz, bx, piece))
        if nx == 4:
            ahead = lax.ppermute(piece, "x", [(k, (k + 1) % nx) for k in range(nx)])
            behind = lax.ppermute(piece, "x", [(k, (k - 1) % nx) for k in range(nx)])
            onward = jnp.where(c == 0, ahead, behind)
            pairs = [(k * 2, ((k + 1) % nx) * 2) for k in range(nx)]
            pairs += [(k * 2 + 1, ((k - 1) % nx) * 2 + 1) for k in range(nx)]
            far = lax.ppermute(onward, ("x", "c"), pairs)
            reached.append((bz, (bx - 1) % nx, ahead))
            reached.append((bz, (bx + 1) % nx, behind))
            reached.append((bz, (bx + 2) % nx, far))
        else:
            for s in range(1, nx):
                moved = lax.ppermute(piece, "x", [(k, (k + s) % nx) for k in range(nx)])
                reached.append((bz, (bx - s) % nx, moved))
    return [(bz * nx + bx, piece) for bz, bx, piece in reached]


def relay_onward(rows_now):
    halves = lax.axis_size("zh")
    sections = lax.axis_size("segment")
    zh = lax.axis_index("zh")
    split = rows_now.reshape((halves, -1) + rows_now.shape[1:])
    local = lax.all_to_all(split, ("x", "c"), split_axis=1, concat_axis=1, tiled=True)
    stay = jnp.where(zh == 0, local[0], local[1])
    cross = jnp.where(zh == 0, local[1], local[0])
    to = lambda s, h: s * halves + h
    stay = lax.ppermute(
        stay,
        ("segment", "zh"),
        [(to(s, h), to((s + 1) % sections, h)) for s in range(sections) for h in range(halves)],
    )
    cross = lax.ppermute(
        cross,
        ("segment", "zh"),
        [(to(s, h), to((s + 1) % sections, 1 - h)) for s in range(sections) for h in range(halves)],
    )
    return jnp.where(
        zh == 0, jnp.concatenate([stay, cross], axis=0), jnp.concatenate([cross, stay], axis=0)
    )


def on_device(latents, w_qkv, w_out, mod_shift, mod_scale, mod_gate, counts):
    frames = lax.axis_size(SEQ)
    patches = latents.shape[2]
    narrow = latents.shape[3]
    span = patches // frames
    segment_rows = latents[0, 0]
    gathered = lax.all_gather(latents, "mp", axis=3, tiled=True)[0, 0]
    widened = gathered.astype(jnp.float32)
    average = jnp.mean(widened, axis=-1, keepdims=True)
    centred = widened - average
    variance = jnp.mean(centred * centred, axis=-1, keepdims=True)
    modulated = (centred * lax.rsqrt(variance + EPS) * mod_scale[0] + mod_shift[0]).astype(
        jnp.bfloat16
    )
    columns = w_qkv.shape[2] * w_qkv.shape[3]
    rows = w_qkv.shape[1]
    payload = jnp.concatenate([w_qkv[0].reshape(rows, columns), w_out[0].T], axis=1)
    arrived = spread_seq(payload)
    core = lax.axis_index("c")
    pair_rows = jnp.concatenate([modulated, swap(modulated, "c")], axis=0)
    w_in = jnp.concatenate([piece[:, :columns] for _, piece in arrived], axis=0)
    reordered = jnp.concatenate(
        [
            lax.dynamic_slice_in_dim(pair_rows, (chip * 2 + core) * rows, rows, axis=1)
            for chip, _ in arrived
        ],
        axis=1,
    )
    both = jnp.dot(reordered, w_in, preferred_element_type=jnp.float32)
    projected = both[:patches] + swap(both[patches:], "c")
    local_heads = w_qkv.shape[3] // HD
    projected = projected.astype(jnp.bfloat16).reshape(patches, 3, local_heads, HD)
    frame_here = seq_index()
    clip_counts = counts[0]
    positions = jnp.arange(frames)

    def spatial(triple):
        count_here = jnp.sum(jnp.where(positions == frame_here, clip_counts, 0))
        usable = jnp.arange(patches) < count_here
        return masked_attention(triple[:, 0], triple[:, 1], triple[:, 2], usable)

    def temporal(triple):
        by_place = triple.reshape(frames, span, 3, local_heads, HD).transpose(1, 0, 2, 3, 4)
        location = frame_here * span + jnp.arange(span)
        usable = location[:, None] < clip_counts[None, :]
        blended = masked_attention(by_place[:, :, 0], by_place[:, :, 1], by_place[:, :, 2], usable)
        return blended.transpose(1, 0, 2, 3).reshape(patches, local_heads, HD)

    attended = lax.cond(lax.axis_index("segment") % 2 == 0, spatial, temporal, projected)
    attended = attended.reshape(patches, local_heads * HD)
    member = lax.axis_index("mp")
    width = w_out.shape[2]
    backs = []
    for chip, piece in arrived:
        back = piece[:, columns:]
        backs.append((chip * 2 + core, back))
        backs.append((chip * 2 + 1 - core, swap(back, "c")))
    w_back = jnp.concatenate([back for _, back in backs], axis=0)
    mixed = jnp.einsum(
        "tr,cr->tc", attended, w_back, preferred_element_type=jnp.float32
    ).astype(jnp.bfloat16)
    partials = jnp.zeros((patches, width * frames), jnp.bfloat16)
    for slot, (where, _) in enumerate(backs):
        partials = lax.dynamic_update_slice_in_dim(
            partials, mixed[:, slot * width : (slot + 1) * width], where * width, axis=1
        )
    summed = lax.psum_scatter(partials, "mp", scatter_dimension=1, tiled=True).astype(
        jnp.float32
    )
    gate_here = lax.dynamic_slice_in_dim(mod_gate[0], member * narrow, narrow)
    updated = (segment_rows.astype(jnp.float32) + gate_here * summed).astype(jnp.bfloat16)
    updated = updated.reshape(frames, span, narrow)
    moved = relay_onward(updated)
    return moved.reshape(1, 1, patches, narrow)


def solution(mesh):
    seg, seq, mp = mesh.devices.shape
    inner = mesh.devices.reshape(seg, 2, seq // 4, 2, mp)
    fine = jax.sharding.Mesh(inner, ("segment", "zh", "x", "c", "mp"))
    return jax.shard_map(
        on_device,
        mesh=fine,
        in_specs=(
            P("segment", SEQ, None, "mp"),
            P("segment", SEQ, None, "mp"),
            P("segment", "mp", SEQ),
            P("segment", None),
            P("segment", None),
            P("segment", None),
            P("segment", None),
        ),
        out_specs=P("segment", SEQ, None, "mp"),
        check_vma=False,
    )
```

```python
import math

import jax
import jax.numpy as jnp
from jax import lax
from jax.sharding import PartitionSpec as P


HD = 128


EPS = 1e-06
NEG_FILL = -1e30


def masked_attention(queries, keys_in, values, usable):
    factor = 1.0 / math.sqrt(queries.shape[-1])
    scores = (
        jnp.einsum("...ihe,...jhe->...hij", queries, keys_in, preferred_element_type=jnp.float32)
        * factor
    )
    allowed = usable[..., None, :, None] & usable[..., None, None, :]
    masked = jnp.where(allowed, scores, NEG_FILL)
    highest = jnp.max(masked, axis=-1, keepdims=True)
    raised = jnp.where(allowed, jnp.exp(masked - highest), 0.0)
    spare_one = jnp.where(usable, 0.0, 1.0)[..., None, :, None]
    weights = (raised / (jnp.sum(raised, axis=-1, keepdims=True) + spare_one)).astype(jnp.bfloat16)
    blended = jnp.einsum(
        "...hij,...jhe->...ihe", weights, values, preferred_element_type=jnp.float32
    )
    return blended.astype(jnp.bfloat16)


SEQ = ("zh", "x", "c")


def seq_index():
    return (lax.axis_index("zh") * lax.axis_size("x") + lax.axis_index("x")) * lax.axis_size(
        "c"
    ) + lax.axis_index("c")


def swap(block, axis):
    return lax.ppermute(block, axis, [(0, 1), (1, 0)])


def spread_seq(block, z_chunks=2):
    zh = lax.axis_index("zh")
    x = lax.axis_index("x")
    c = lax.axis_index("c")
    nx = lax.axis_size("x")
    step = block.shape[0] // z_chunks
    held = [(zh, x, 0, block)]
    for k in range(z_chunks):
        part = swap(block[k * step : (k + 1) * step], "zh")
        held.append((1 - zh, x, k * step, part))
    reached = []
    for bz, bx, first, piece in held:
        reached.append((bz, bx, first, piece))
        if nx == 4:
            ahead = lax.ppermute(piece, "x", [(k, (k + 1) % nx) for k in range(nx)])
            behind = lax.ppermute(piece, "x", [(k, (k - 1) % nx) for k in range(nx)])
            onward = jnp.where(c == 0, ahead, behind)
            pairs = [(k * 2, ((k + 1) % nx) * 2) for k in range(nx)]
            pairs += [(k * 2 + 1, ((k - 1) % nx) * 2 + 1) for k in range(nx)]
            far = lax.ppermute(onward, ("x", "c"), pairs)
            reached.append((bz, (bx - 1) % nx, first, ahead))
            reached.append((bz, (bx + 1) % nx, first, behind))
            reached.append((bz, (bx + 2) % nx, first, far))
        else:
            for s in range(1, nx):
                moved = lax.ppermute(piece, "x", [(k, (k + s) % nx) for k in range(nx)])
                reached.append((bz, (bx - s) % nx, first, moved))
    return [(bz * nx + bx, first, piece) for bz, bx, first, piece in reached]


def relay_onward(rows_now):
    halves = lax.axis_size("zh")
    sections = lax.axis_size("segment")
    zh = lax.axis_index("zh")
    split = rows_now.reshape((halves, -1) + rows_now.shape[1:])
    local = lax.all_to_all(split, ("x", "c"), split_axis=1, concat_axis=1, tiled=True)
    stay = jnp.where(zh == 0, local[0], local[1])
    cross = jnp.where(zh == 0, local[1], local[0])
    to = lambda s, h: s * halves + h
    stay = lax.ppermute(
        stay,
        ("segment", "zh"),
        [(to(s, h), to((s + 1) % sections, h)) for s in range(sections) for h in range(halves)],
    )
    cross = lax.ppermute(
        cross,
        ("segment", "zh"),
        [(to(s, h), to((s + 1) % sections, 1 - h)) for s in range(sections) for h in range(halves)],
    )
    return jnp.where(
        zh == 0, jnp.concatenate([stay, cross], axis=0), jnp.concatenate([cross, stay], axis=0)
    )


def on_device(latents, w_qkv, w_out, mod_shift, mod_scale, mod_gate, counts):
    frames = lax.axis_size(SEQ)
    patches = latents.shape[2]
    narrow = latents.shape[3]
    span = patches // frames
    segment_rows = latents[0, 0]
    gathered = lax.all_gather(latents, "mp", axis=3, tiled=True)[0, 0]
    widened = gathered.astype(jnp.float32)
    average = jnp.mean(widened, axis=-1, keepdims=True)
    centred = widened - average
    variance = jnp.mean(centred * centred, axis=-1, keepdims=True)
    modulated = (centred * lax.rsqrt(variance + EPS) * mod_scale[0] + mod_shift[0]).astype(
        jnp.bfloat16
    )
    columns = w_qkv.shape[2] * w_qkv.shape[3]
    rows = w_qkv.shape[1]
    payload = jnp.concatenate([w_qkv[0].reshape(rows, columns), w_out[0].T], axis=1)
    arrived = spread_seq(payload)
    core = lax.axis_index("c")
    pair_rows = jnp.concatenate([modulated, swap(modulated, "c")], axis=0)
    w_in = jnp.concatenate([piece[:, :columns] for _, _, piece in arrived], axis=0)
    reordered = jnp.concatenate(
        [
            lax.dynamic_slice_in_dim(
                pair_rows, (chip * 2 + core) * rows + first, piece.shape[0], axis=1
            )
            for chip, first, piece in arrived
        ],
        axis=1,
    )
    both = jnp.dot(reordered, w_in, preferred_element_type=jnp.float32)
    projected = both[:patches] + swap(both[patches:], "c")
    local_heads = w_qkv.shape[3] // HD
    projected = projected.astype(jnp.bfloat16).reshape(patches, 3, local_heads, HD)
    frame_here = seq_index()
    clip_counts = counts[0]
    positions = jnp.arange(frames)

    def spatial(triple):
        count_here = jnp.sum(jnp.where(positions == frame_here, clip_counts, 0))
        usable = jnp.arange(patches) < count_here
        return masked_attention(triple[:, 0], triple[:, 1], triple[:, 2], usable)

    def temporal(triple):
        by_place = triple.reshape(frames, span, 3, local_heads, HD).transpose(1, 0, 2, 3, 4)
        location = frame_here * span + jnp.arange(span)
        usable = location[:, None] < clip_counts[None, :]
        blended = masked_attention(by_place[:, :, 0], by_place[:, :, 1], by_place[:, :, 2], usable)
        return blended.transpose(1, 0, 2, 3).reshape(patches, local_heads, HD)

    attended = lax.cond(lax.axis_index("segment") % 2 == 0, spatial, temporal, projected)
    attended = attended.reshape(patches, local_heads * HD)
    member = lax.axis_index("mp")
    width = w_out.shape[2]
    pair_att = jnp.concatenate([attended, swap(attended, "c")], axis=0)
    w_back = jnp.concatenate([piece[:, columns:] for _, _, piece in arrived], axis=0)
    mixed = jnp.einsum(
        "tr,cr->tc", pair_att, w_back, preferred_element_type=jnp.float32
    ).astype(jnp.bfloat16)
    partials = jnp.zeros((2 * patches, width * frames // 2), jnp.bfloat16)
    slot = 0
    for chip, first, piece in arrived:
        size = piece.shape[0]
        partials = lax.dynamic_update_slice_in_dim(
            partials, mixed[:, slot : slot + size], chip * width + first, axis=1
        )
        slot += size
    pair_sum = lax.psum_scatter(partials, "mp", scatter_dimension=1, tiled=True)
    mine = pair_sum[:patches]
    theirs = swap(pair_sum[patches:], "c")
    summed = jnp.where(
        core == 0,
        jnp.concatenate([mine, theirs], axis=1),
        jnp.concatenate([theirs, mine], axis=1),
    ).astype(jnp.float32)
    gate_here = lax.dynamic_slice_in_dim(mod_gate[0], member * narrow, narrow)
    updated = (segment_rows.astype(jnp.float32) + gate_here * summed).astype(jnp.bfloat16)
    updated = updated.reshape(frames, span, narrow)
    moved = relay_onward(updated)
    return moved.reshape(1, 1, patches, narrow)


def solution(mesh):
    seg, seq, mp = mesh.devices.shape
    inner = mesh.devices.reshape(seg, 2, seq // 4, 2, mp)
    fine = jax.sharding.Mesh(inner, ("segment", "zh", "x", "c", "mp"))
    return jax.shard_map(
        on_device,
        mesh=fine,
        in_specs=(
            P("segment", SEQ, None, "mp"),
            P("segment", SEQ, None, "mp"),
            P("segment", "mp", SEQ),
            P("segment", None),
            P("segment", None),
            P("segment", None),
            P("segment", None),
        ),
        out_specs=P("segment", SEQ, None, "mp"),
        check_vma=False,
    )
```

```python
import math

import jax
import jax.numpy as jnp
from jax import lax
from jax.sharding import PartitionSpec as P


HD = 128


EPS = 1e-06
NEG_FILL = -1e30


def masked_attention(queries, keys_in, values, usable):
    factor = 1.0 / math.sqrt(queries.shape[-1])
    scores = (
        jnp.einsum("...ihe,...jhe->...hij", queries, keys_in, preferred_element_type=jnp.float32)
        * factor
    )
    allowed = usable[..., None, :, None] & usable[..., None, None, :]
    masked = jnp.where(allowed, scores, NEG_FILL)
    highest = jnp.max(masked, axis=-1, keepdims=True)
    raised = jnp.where(allowed, jnp.exp(masked - highest), 0.0)
    spare_one = jnp.where(usable, 0.0, 1.0)[..., None, :, None]
    weights = (raised / (jnp.sum(raised, axis=-1, keepdims=True) + spare_one)).astype(jnp.bfloat16)
    blended = jnp.einsum(
        "...hij,...jhe->...ihe", weights, values, preferred_element_type=jnp.float32
    )
    return blended.astype(jnp.bfloat16)


SEQ = ("zh", "x", "c")


def seq_index():
    return (lax.axis_index("zh") * lax.axis_size("x") + lax.axis_index("x")) * lax.axis_size(
        "c"
    ) + lax.axis_index("c")


def swap(block, axis):
    return lax.ppermute(block, axis, [(0, 1), (1, 0)])


def spread_seq(block):
    zh = lax.axis_index("zh")
    x = lax.axis_index("x")
    c = lax.axis_index("c")
    nx = lax.axis_size("x")
    held = [(zh, x, block), (1 - zh, x, swap(block, "zh"))]
    reached = []
    for bz, bx, piece in held:
        reached.append((bz, bx, piece))
        if nx == 4:
            ahead = lax.ppermute(piece, "x", [(k, (k + 1) % nx) for k in range(nx)])
            behind = lax.ppermute(piece, "x", [(k, (k - 1) % nx) for k in range(nx)])
            onward = jnp.where(c == 0, ahead, behind)
            pairs = [(k * 2, ((k + 1) % nx) * 2) for k in range(nx)]
            pairs += [(k * 2 + 1, ((k - 1) % nx) * 2 + 1) for k in range(nx)]
            far = lax.ppermute(onward, ("x", "c"), pairs)
            reached.append((bz, (bx - 1) % nx, ahead))
            reached.append((bz, (bx + 1) % nx, behind))
            reached.append((bz, (bx + 2) % nx, far))
        else:
            for s in range(1, nx):
                moved = lax.ppermute(piece, "x", [(k, (k + s) % nx) for k in range(nx)])
                reached.append((bz, (bx - s) % nx, moved))
    return [(bz * nx + bx, piece) for bz, bx, piece in reached]


def relay_onward(rows_now):
    halves = lax.axis_size("zh")
    sections = lax.axis_size("segment")
    zh = lax.axis_index("zh")
    split = rows_now.reshape((halves, -1) + rows_now.shape[1:])
    local = lax.all_to_all(split, ("x", "c"), split_axis=1, concat_axis=1, tiled=True)
    stay = jnp.where(zh == 0, local[0], local[1])
    cross = jnp.where(zh == 0, local[1], local[0])
    to = lambda s, h: s * halves + h
    stay = lax.ppermute(
        stay,
        ("segment", "zh"),
        [(to(s, h), to((s + 1) % sections, h)) for s in range(sections) for h in range(halves)],
    )
    cross = lax.ppermute(
        cross,
        ("segment", "zh"),
        [(to(s, h), to((s + 1) % sections, 1 - h)) for s in range(sections) for h in range(halves)],
    )
    return jnp.where(
        zh == 0, jnp.concatenate([stay, cross], axis=0), jnp.concatenate([cross, stay], axis=0)
    )


def on_device(latents, w_qkv, w_out, mod_shift, mod_scale, mod_gate, counts):
    frames = lax.axis_size(SEQ)
    patches = latents.shape[2]
    narrow = latents.shape[3]
    span = patches // frames
    segment_rows = latents[0, 0]
    gathered = lax.all_gather(latents, "mp", axis=3, tiled=True)[0, 0]
    widened = gathered.astype(jnp.float32)
    average = jnp.mean(widened, axis=-1, keepdims=True)
    centred = widened - average
    variance = jnp.mean(centred * centred, axis=-1, keepdims=True)
    modulated = (centred * lax.rsqrt(variance + EPS) * mod_scale[0] + mod_shift[0]).astype(
        jnp.bfloat16
    )
    columns = w_qkv.shape[2] * w_qkv.shape[3]
    rows = w_qkv.shape[1]
    payload = jnp.concatenate([w_qkv[0].reshape(rows, columns), w_out[0].T], axis=1)
    arrived = spread_seq(payload)
    core = lax.axis_index("c")
    pair_rows = jnp.concatenate([modulated, swap(modulated, "c")], axis=0)
    w_in = jnp.concatenate([piece[:, :columns] for _, piece in arrived], axis=0)
    reordered = jnp.concatenate(
        [
            lax.dynamic_slice_in_dim(pair_rows, (chip * 2 + core) * rows, rows, axis=1)
            for chip, _ in arrived
        ],
        axis=1,
    )
    both = jnp.dot(reordered, w_in, preferred_element_type=jnp.float32)
    projected = both[:patches] + swap(both[patches:].astype(jnp.bfloat16), "c").astype(
        jnp.float32
    )
    local_heads = w_qkv.shape[3] // HD
    projected = projected.astype(jnp.bfloat16).reshape(patches, 3, local_heads, HD)
    frame_here = seq_index()
    clip_counts = counts[0]
    positions = jnp.arange(frames)

    def spatial(triple):
        count_here = jnp.sum(jnp.where(positions == frame_here, clip_counts, 0))
        usable = jnp.arange(patches) < count_here
        return masked_attention(triple[:, 0], triple[:, 1], triple[:, 2], usable)

    def temporal(triple):
        by_place = triple.reshape(frames, span, 3, local_heads, HD).transpose(1, 0, 2, 3, 4)
        location = frame_here * span + jnp.arange(span)
        usable = location[:, None] < clip_counts[None, :]
        blended = masked_attention(by_place[:, :, 0], by_place[:, :, 1], by_place[:, :, 2], usable)
        return blended.transpose(1, 0, 2, 3).reshape(patches, local_heads, HD)

    attended = lax.cond(lax.axis_index("segment") % 2 == 0, spatial, temporal, projected)
    attended = attended.reshape(patches, local_heads * HD)
    member = lax.axis_index("mp")
    width = w_out.shape[2]
    pair_att = jnp.concatenate([attended, swap(attended, "c")], axis=0)
    w_back = jnp.concatenate([piece[:, columns:] for _, piece in arrived], axis=0)
    mixed = jnp.einsum(
        "tr,cr->tc", pair_att, w_back, preferred_element_type=jnp.float32
    ).astype(jnp.bfloat16)
    partials = jnp.zeros((2 * patches, width * frames // 2), jnp.bfloat16)
    for slot, (chip, _) in enumerate(arrived):
        partials = lax.dynamic_update_slice_in_dim(
            partials, mixed[:, slot * width : (slot + 1) * width], chip * width, axis=1
        )
    pair_sum = lax.psum_scatter(partials, "mp", scatter_dimension=1, tiled=True)
    mine = pair_sum[:patches]
    theirs = swap(pair_sum[patches:], "c")
    summed = jnp.where(
        core == 0,
        jnp.concatenate([mine, theirs], axis=1),
        jnp.concatenate([theirs, mine], axis=1),
    ).astype(jnp.float32)
    gate_here = lax.dynamic_slice_in_dim(mod_gate[0], member * narrow, narrow)
    updated = (segment_rows.astype(jnp.float32) + gate_here * summed).astype(jnp.bfloat16)
    updated = updated.reshape(frames, span, narrow)
    moved = relay_onward(updated)
    return moved.reshape(1, 1, patches, narrow)


def solution(mesh):
    seg, seq, mp = mesh.devices.shape
    inner = mesh.devices.reshape(seg, 2, seq // 4, 2, mp)
    fine = jax.sharding.Mesh(inner, ("segment", "zh", "x", "c", "mp"))
    return jax.shard_map(
        on_device,
        mesh=fine,
        in_specs=(
            P("segment", SEQ, None, "mp"),
            P("segment", SEQ, None, "mp"),
            P("segment", "mp", SEQ),
            P("segment", None),
            P("segment", None),
            P("segment", None),
            P("segment", None),
        ),
        out_specs=P("segment", SEQ, None, "mp"),
        check_vma=False,
    )
```

```python
import math

import jax
import jax.numpy as jnp
from jax import lax
from jax.sharding import PartitionSpec as P


HD = 128


EPS = 1e-06
NEG_FILL = -1e30


def masked_attention(queries, keys_in, values, usable):
    factor = 1.0 / math.sqrt(queries.shape[-1])
    scores = (
        jnp.einsum("...ihe,...jhe->...hij", queries, keys_in, preferred_element_type=jnp.float32)
        * factor
    )
    allowed = usable[..., None, :, None] & usable[..., None, None, :]
    masked = jnp.where(allowed, scores, NEG_FILL)
    highest = jnp.max(masked, axis=-1, keepdims=True)
    raised = jnp.where(allowed, jnp.exp(masked - highest), 0.0)
    spare_one = jnp.where(usable, 0.0, 1.0)[..., None, :, None]
    weights = (raised / (jnp.sum(raised, axis=-1, keepdims=True) + spare_one)).astype(jnp.bfloat16)
    blended = jnp.einsum(
        "...hij,...jhe->...ihe", weights, values, preferred_element_type=jnp.float32
    )
    return blended.astype(jnp.bfloat16)


SEQ = ("zh", "x", "c")


def seq_index():
    return (lax.axis_index("zh") * lax.axis_size("x") + lax.axis_index("x")) * lax.axis_size(
        "c"
    ) + lax.axis_index("c")


def swap(block, axis):
    return lax.ppermute(block, axis, [(0, 1), (1, 0)])


def spread_seq(block):
    zh = lax.axis_index("zh")
    x = lax.axis_index("x")
    c = lax.axis_index("c")
    nx = lax.axis_size("x")
    held = [(zh, x, block), (1 - zh, x, swap(block, "zh"))]
    reached = []
    for bz, bx, piece in held:
        reached.append((bz, bx, piece))
        if nx == 4:
            ahead = lax.ppermute(piece, "x", [(k, (k + 1) % nx) for k in range(nx)])
            behind = lax.ppermute(piece, "x", [(k, (k - 1) % nx) for k in range(nx)])
            onward = jnp.where(c == 0, ahead, behind)
            pairs = [(k * 2, ((k + 1) % nx) * 2) for k in range(nx)]
            pairs += [(k * 2 + 1, ((k - 1) % nx) * 2 + 1) for k in range(nx)]
            far = lax.ppermute(onward, ("x", "c"), pairs)
            reached.append((bz, (bx - 1) % nx, ahead))
            reached.append((bz, (bx + 1) % nx, behind))
            reached.append((bz, (bx + 2) % nx, far))
        else:
            for s in range(1, nx):
                moved = lax.ppermute(piece, "x", [(k, (k + s) % nx) for k in range(nx)])
                reached.append((bz, (bx - s) % nx, moved))
    return [(bz * nx + bx, piece) for bz, bx, piece in reached]


def relay_onward(rows_now):
    halves = lax.axis_size("zh")
    sections = lax.axis_size("segment")
    zh = lax.axis_index("zh")
    split = rows_now.reshape((halves, -1) + rows_now.shape[1:])
    local = lax.all_to_all(split, ("x", "c"), split_axis=1, concat_axis=1, tiled=True)
    stay = jnp.where(zh == 0, local[0], local[1])
    cross = jnp.where(zh == 0, local[1], local[0])
    to = lambda s, h: s * halves + h
    stay = lax.ppermute(
        stay,
        ("segment", "zh"),
        [(to(s, h), to((s + 1) % sections, h)) for s in range(sections) for h in range(halves)],
    )
    cross = lax.ppermute(
        cross,
        ("segment", "zh"),
        [(to(s, h), to((s + 1) % sections, 1 - h)) for s in range(sections) for h in range(halves)],
    )
    return jnp.where(
        zh == 0, jnp.concatenate([stay, cross], axis=0), jnp.concatenate([cross, stay], axis=0)
    )


def on_device(latents, w_qkv, w_out, mod_shift, mod_scale, mod_gate, counts):
    frames = lax.axis_size(SEQ)
    patches = latents.shape[2]
    narrow = latents.shape[3]
    span = patches // frames
    segment_rows = latents[0, 0]
    gathered = lax.all_gather(latents, "mp", axis=3, tiled=True)[0, 0]
    widened = gathered.astype(jnp.float32)
    average = jnp.mean(widened, axis=-1, keepdims=True)
    centred = widened - average
    variance = jnp.mean(centred * centred, axis=-1, keepdims=True)
    modulated = (centred * lax.rsqrt(variance + EPS) * mod_scale[0] + mod_shift[0]).astype(
        jnp.bfloat16
    )
    columns = w_qkv.shape[2] * w_qkv.shape[3]
    rows = w_qkv.shape[1]
    payload = jnp.concatenate([w_qkv[0].reshape(rows, columns), w_out[0].T], axis=1)
    arrived = spread_seq(payload)
    core = lax.axis_index("c")
    pair_rows = jnp.concatenate([modulated, swap(modulated, "c")], axis=0)
    both = None
    for group in (arrived[:4], arrived[4:]):
        w_in = jnp.concatenate([piece[:, :columns] for _, piece in group], axis=0)
        reordered = jnp.concatenate(
            [
                lax.dynamic_slice_in_dim(pair_rows, (chip * 2 + core) * rows, rows, axis=1)
                for chip, _ in group
            ],
            axis=1,
        )
        part = jnp.dot(reordered, w_in, preferred_element_type=jnp.float32)
        both = part if both is None else both + part
    projected = both[:patches] + swap(both[patches:].astype(jnp.bfloat16), "c").astype(
        jnp.float32
    )
    local_heads = w_qkv.shape[3] // HD
    projected = projected.astype(jnp.bfloat16).reshape(patches, 3, local_heads, HD)
    frame_here = seq_index()
    clip_counts = counts[0]
    positions = jnp.arange(frames)

    def spatial(triple):
        count_here = jnp.sum(jnp.where(positions == frame_here, clip_counts, 0))
        usable = jnp.arange(patches) < count_here
        return masked_attention(triple[:, 0], triple[:, 1], triple[:, 2], usable)

    def temporal(triple):
        by_place = triple.reshape(frames, span, 3, local_heads, HD).transpose(1, 0, 2, 3, 4)
        location = frame_here * span + jnp.arange(span)
        usable = location[:, None] < clip_counts[None, :]
        blended = masked_attention(by_place[:, :, 0], by_place[:, :, 1], by_place[:, :, 2], usable)
        return blended.transpose(1, 0, 2, 3).reshape(patches, local_heads, HD)

    attended = lax.cond(lax.axis_index("segment") % 2 == 0, spatial, temporal, projected)
    attended = attended.reshape(patches, local_heads * HD)
    member = lax.axis_index("mp")
    width = w_out.shape[2]
    pair_att = jnp.concatenate([attended, swap(attended, "c")], axis=0)
    w_back = jnp.concatenate([piece[:, columns:] for _, piece in arrived], axis=0)
    mixed = jnp.einsum(
        "tr,cr->tc", pair_att, w_back, preferred_element_type=jnp.float32
    ).astype(jnp.bfloat16)
    partials = jnp.zeros((2 * patches, width * frames // 2), jnp.bfloat16)
    for slot, (chip, _) in enumerate(arrived):
        partials = lax.dynamic_update_slice_in_dim(
            partials, mixed[:, slot * width : (slot + 1) * width], chip * width, axis=1
        )
    pair_sum = lax.psum_scatter(partials, "mp", scatter_dimension=1, tiled=True)
    mine = pair_sum[:patches]
    theirs = swap(pair_sum[patches:], "c")
    summed = jnp.where(
        core == 0,
        jnp.concatenate([mine, theirs], axis=1),
        jnp.concatenate([theirs, mine], axis=1),
    ).astype(jnp.float32)
    gate_here = lax.dynamic_slice_in_dim(mod_gate[0], member * narrow, narrow)
    updated = (segment_rows.astype(jnp.float32) + gate_here * summed).astype(jnp.bfloat16)
    updated = updated.reshape(frames, span, narrow)
    moved = relay_onward(updated)
    return moved.reshape(1, 1, patches, narrow)


def solution(mesh):
    seg, seq, mp = mesh.devices.shape
    inner = mesh.devices.reshape(seg, 2, seq // 4, 2, mp)
    fine = jax.sharding.Mesh(inner, ("segment", "zh", "x", "c", "mp"))
    return jax.shard_map(
        on_device,
        mesh=fine,
        in_specs=(
            P("segment", SEQ, None, "mp"),
            P("segment", SEQ, None, "mp"),
            P("segment", "mp", SEQ),
            P("segment", None),
            P("segment", None),
            P("segment", None),
            P("segment", None),
        ),
        out_specs=P("segment", SEQ, None, "mp"),
        check_vma=False,
    )
```
